768 devices in a mesh: section: 64 (over z_lo, y, core), tp: 12 (over x, z_hi).
Axes of the slice: x: 4, y: 8, z: 12 (z_hi: 3, z_lo: 4; z = z_hi * 4 + z_lo), core: 2. Of those that a mesh axis runs over, the one named last changes fastest.
Arguments:
- saved_inputs: bfloat16 [2, 64, 1536, 4608], P(None, 'section', 'tp'), may hold values from -10.5 to 10.5
- incoming: bfloat16 [64, 1536, 4608], P('section', 'tp'), may hold values from -6 to 6
- qk_gain: float32 [64, 4608], P('section'), may hold values from -1 to 1
- value_gain: float32 [64, 4608], P('section'), may hold values from -1 to 1
Outputs:
- passed: bfloat16 [64, 1536, 4608], P('section', 'tp')
- qk_gain_grad: float32 [64, 4608], P('section', 'tp')
- value_gain_grad: float32 [64, 4608], P('section', 'tp')
The draws below stay inside these ranges and needn't reach their ends.
All inputs are finite; a program needn't handle non-finite values.
Results may differ from the reference program's by a relative error of at most 0.0079.
Values may be sent and summed in bfloat16 or wider, within the bound.
No kernel may reach another device: no remote copies, remote signals or barrier semaphores. Data moves between devices by JAX's collectives and lax.ppermute only.
A program may use at most 64 MiB of HBM per device.

```python
import jax
import jax.numpy as jnp
from jax import lax

HEADS = 36
HEAD_DIM = 128
TICKS = 2
D = 4608
SEQ_LEN = 256
TOKENS = 1536
N_SECTION = 64


def draw_saved_inputs(key, part):
    shape_full = (TICKS, N_SECTION, TOKENS, D)
    base_key = jax.random.fold_in(key, 0)
    baseline = jax.random.truncated_normal(base_key, -6.0, 6.0, shape_full, jnp.float32)
    return baseline.astype(jnp.bfloat16)


def steps_of(own_key, extent, cuts, smallest, high):
    level = 1.0
    for dim, shards_of in cuts:
        draws = jax.random.uniform(jax.random.fold_in(jax.random.fold_in(own_key, 6), dim), (shards_of,), jnp.float32, smallest / len(cuts), high / len(cuts))
        level = level * jnp.repeat(jnp.exp(draws), extent[dim] // shards_of).reshape((-1,) + (1,) * (len(extent) - 1 - dim))
    return level


def bell_draw(own_key, shape, width, most, cuts=(), held_as=jnp.bfloat16):
    factor_of = steps_of(own_key, shape, cuts, -0.22, 0.18) if cuts else 1.0
    values = jax.random.normal(own_key, shape, jnp.float32) * width * factor_of
    return jnp.minimum(jnp.maximum(values, -most), most).astype(held_as)


def setup_inputs(seed: int = 0) -> dict:
    key_of = jax.random.split(jax.random.key(seed), 5)
    return {
        "saved_inputs": draw_saved_inputs(jax.random.fold_in(key_of[4], 71), 0),
        "incoming": bell_draw(key_of[1], (N_SECTION, TOKENS, D), 1.0, 6.0, ((0, 64), (1, 12))),
        "qk_gain": jnp.clip(jax.random.uniform(key_of[2], (N_SECTION, D), jnp.float32, -1.0, 1.0) * steps_of(key_of[2], (N_SECTION, D), ((0, 64),), -0.4, 0.0), -1.0, 1.0),
        "value_gain": jnp.clip(jax.random.uniform(key_of[3], (N_SECTION, D), jnp.float32, -1.0, 1.0) * steps_of(key_of[3], (N_SECTION, D), ((0, 64),), -0.4, 0.0), -1.0, 1.0),
    }


def attend_grads(queries, keys, values, upstream, allowed, scale):
    scores = jnp.einsum('nqhe,nkhe->nhqk', queries, keys) * scale
    scores = jnp.where(allowed, scores, -jnp.inf)
    row_max = jnp.max(scores, axis=-1, keepdims=True)
    weights = jnp.exp(scores - row_max)
    probs = weights / jnp.sum(weights, axis=-1, keepdims=True)
    probs_low = lax.optimization_barrier(probs.astype(jnp.bfloat16)).astype(jnp.float32)
    prob_grad = jnp.einsum('nqhe,nkhe->nhqk', upstream, values)
    score_grad = probs * (prob_grad - jnp.sum(probs * prob_grad, axis=-1, keepdims=True))
    score_low = lax.optimization_barrier(score_grad.astype(jnp.bfloat16)).astype(jnp.float32)
    query_grad = jnp.einsum('nhqk,nkhe->nqhe', score_low, keys) * scale
    key_grad = jnp.einsum('nhqk,nqhe->nkhe', score_low, queries) * scale
    value_grad = jnp.einsum('nhqk,nqhe->nkhe', probs_low, upstream)
    return query_grad, key_grad, value_grad


def section_tick(inputs, upstream, gain_qk, gain_value):
    row_total = inputs.shape[0]
    count = row_total // SEQ_LEN
    wide = inputs.astype(jnp.float32)
    keys = lax.optimization_barrier((wide * gain_qk).astype(jnp.bfloat16)).astype(jnp.float32)
    values = lax.optimization_barrier((wide * gain_value).astype(jnp.bfloat16)).astype(jnp.float32)
    shape_four = (count, SEQ_LEN, HEADS, HEAD_DIM)
    upstream_wide = upstream.astype(jnp.float32)
    allowed = jnp.tril(jnp.ones((SEQ_LEN, SEQ_LEN), dtype=bool))
    query_grad, key_grad, value_grad = attend_grads(
        keys.reshape(shape_four), keys.reshape(shape_four), values.reshape(shape_four),
        upstream_wide.reshape(shape_four), allowed, HEAD_DIM ** -0.5)
    qk_total = (query_grad + key_grad).reshape(row_total, D)
    value_total = value_grad.reshape(row_total, D)
    grad_in = (upstream_wide + qk_total * gain_qk + value_total * gain_value).astype(jnp.bfloat16)
    return grad_in, jnp.sum(wide * qk_total, axis=0), jnp.sum(wide * value_total, axis=0)


def reference(saved_inputs, incoming, qk_gain, value_gain):
    upstream = incoming
    qk_sum = jnp.zeros((N_SECTION, D), jnp.float32)
    value_sum = jnp.zeros((N_SECTION, D), jnp.float32)
    for tick_index in range(TICKS):
        grad_in, qk_part, value_part = lax.map(
            lambda section_items: section_tick(*section_items),
            (saved_inputs[tick_index], upstream, qk_gain, value_gain))
        qk_sum = qk_sum + qk_part
        value_sum = value_sum + value_part
        upstream = jnp.roll(grad_in, -1, axis=0)
    return upstream, qk_sum, value_sum
```

```python
import jax
import jax.numpy as jnp
from jax import lax
from jax.sharding import PartitionSpec as P

HEAD_DIM = 128
SEQ_LEN = 256


def from_behind(block, axis, distance):
    devices = range(lax.axis_size(axis))
    route = [((i - distance) % len(devices), i) for i in devices]
    return lax.ppermute(block, axis, route)


def attend_grads(queries, keys, values, upstream, allowed, scale):
    scores = (
        jnp.einsum("nqhe,nkhe->nhqk", queries, keys, preferred_element_type=jnp.float32) * scale
    )
    scores = jnp.where(allowed, scores, -jnp.inf)
    row_max = jnp.max(scores, axis=-1, keepdims=True)
    weights = jnp.exp(scores - row_max)
    probs = weights / jnp.sum(weights, axis=-1, keepdims=True)
    probs_low = probs.astype(jnp.bfloat16)
    prob_grad = jnp.einsum("nqhe,nkhe->nhqk", upstream, values, preferred_element_type=jnp.float32)
    score_grad = probs * (prob_grad - jnp.sum(probs * prob_grad, axis=-1, keepdims=True))
    score_low = score_grad.astype(jnp.bfloat16)
    query_grad = (
        jnp.einsum("nhqk,nkhe->nqhe", score_low, keys, preferred_element_type=jnp.float32) * scale
    )
    key_grad = (
        jnp.einsum("nhqk,nqhe->nkhe", score_low, queries, preferred_element_type=jnp.float32)
        * scale
    )
    value_grad = jnp.einsum(
        "nhqk,nqhe->nkhe", probs_low, upstream, preferred_element_type=jnp.float32
    )
    return (query_grad, key_grad, value_grad)


def pass_on(grad_in):
    return from_behind(grad_in, "section", -1)


def local_backward(inputs, upstream, gain_qk, gain_value):
    row_total = inputs.shape[0]
    local_width = inputs.shape[1]
    count = row_total // SEQ_LEN
    local_heads = local_width // HEAD_DIM
    wide = inputs.astype(jnp.float32)
    keys = (wide * gain_qk).astype(jnp.bfloat16)
    values = (wide * gain_value).astype(jnp.bfloat16)
    shape_four = (count, SEQ_LEN, local_heads, HEAD_DIM)
    allowed = jnp.tril(jnp.ones((SEQ_LEN, SEQ_LEN), dtype=bool))
    query_grad, key_grad, value_grad = attend_grads(
        keys.reshape(shape_four),
        keys.reshape(shape_four),
        values.reshape(shape_four),
        upstream.reshape(shape_four),
        allowed,
        HEAD_DIM ** (-0.5),
    )
    qk_total = (query_grad + key_grad).reshape(row_total, local_width)
    value_total = value_grad.reshape(row_total, local_width)
    grad_in = (upstream.astype(jnp.float32) + qk_total * gain_qk + value_total * gain_value).astype(
        jnp.bfloat16
    )
    return (grad_in, jnp.sum(wide * qk_total, axis=0), jnp.sum(wide * value_total, axis=0))


def to_heads(block):
    return lax.all_to_all(block, "tp", split_axis=block.ndim - 1, concat_axis=block.ndim - 2, tiled=True)


def shards(saved_inputs, incoming, qk_gain, value_gain):
    tick_count = saved_inputs.shape[0]
    local_width = qk_gain.shape[1] // lax.axis_size("tp")
    offset = lax.axis_index("tp") * local_width
    gain_qk = lax.dynamic_slice_in_dim(qk_gain[0], offset, local_width)
    gain_value = lax.dynamic_slice_in_dim(value_gain[0], offset, local_width)
    first = to_heads(jnp.stack([saved_inputs[0, 0], incoming[0]]))
    inputs_heads = [first[0]] + [to_heads(saved_inputs[t, 0]) for t in range(1, tick_count)]
    upstream = first[1]
    qk_sum = jnp.zeros((local_width,), jnp.float32)
    value_sum = jnp.zeros((local_width,), jnp.float32)
    for tick_index in range(tick_count):
        grad_in, qk_part, value_part = local_backward(
            inputs_heads[tick_index], upstream, gain_qk, gain_value
        )
        qk_sum = qk_sum + qk_part
        value_sum = value_sum + value_part
        upstream = pass_on(grad_in)
    passed = lax.all_to_all(upstream, "tp", split_axis=0, concat_axis=1, tiled=True)
    return (passed[None], qk_sum[None], value_sum[None])


def solution(mesh):
    return jax.shard_map(
        shards,
        mesh=mesh,
        in_specs=(
            P(None, "section", "tp", None),
            P("section", "tp", None),
            P("section", None),
            P("section", None),
        ),
        out_specs=(P("section", "tp", None), P("section", "tp"), P("section", "tp")),
        check_vma=False,
    )
```

```python
import jax
import jax.numpy as jnp
from jax import lax
from jax.sharding import PartitionSpec as P
from jax.experimental import pallas as pl

HEAD_DIM = 128
SEQ_LEN = 256


def from_behind(block, axis, distance):
    devices = range(lax.axis_size(axis))
    route = [((i - distance) % len(devices), i) for i in devices]
    return lax.ppermute(block, axis, route)


def pass_on(grad_in):
    return from_behind(grad_in, "section", -1)


def attention_kernel(x_ref, u_ref, gq_ref, gv_ref, g_ref, qs_ref, vs_ref):
    n = pl.program_id(1)
    scale = HEAD_DIM ** (-0.5)
    wide = x_ref[...].astype(jnp.float32)
    gq = gq_ref[...]
    gv = gv_ref[...]
    keys = (wide * gq).astype(jnp.bfloat16)
    values = (wide * gv).astype(jnp.bfloat16)
    up = u_ref[...]
    nt = (((1,), (1,)), ((), ()))
    tn = (((0,), (0,)), ((), ()))
    scores = lax.dot_general(keys, keys, nt, preferred_element_type=jnp.float32) * scale
    rows = lax.broadcasted_iota(jnp.int32, scores.shape, 0)
    cols = lax.broadcasted_iota(jnp.int32, scores.shape, 1)
    scores = jnp.where(cols <= rows, scores, -jnp.inf)
    row_max = jnp.max(scores, axis=1, keepdims=True)
    weights = jnp.exp(scores - row_max)
    probs = weights / jnp.sum(weights, axis=1, keepdims=True)
    prob_grad = lax.dot_general(up, values, nt, preferred_element_type=jnp.float32)
    score_grad = probs * (prob_grad - jnp.sum(probs * prob_grad, axis=1, keepdims=True))
    score_low = score_grad.astype(jnp.bfloat16)
    probs_low = probs.astype(jnp.bfloat16)
    query_grad = jnp.dot(score_low, keys, preferred_element_type=jnp.float32) * scale
    key_grad = lax.dot_general(score_low, keys, tn, preferred_element_type=jnp.float32) * scale
    value_grad = lax.dot_general(probs_low, up, tn, preferred_element_type=jnp.float32)
    qk_total = query_grad + key_grad
    g_ref[...] = (up.astype(jnp.float32) + qk_total * gq + value_grad * gv).astype(jnp.bfloat16)
    qk_part = jnp.sum(wide * qk_total, axis=0, keepdims=True)
    value_part = jnp.sum(wide * value_grad, axis=0, keepdims=True)

    @pl.when(n == 0)
    def _():
        qs_ref[...] = qk_part
        vs_ref[...] = value_part

    @pl.when(n > 0)
    def _():
        qs_ref[...] += qk_part
        vs_ref[...] += value_part


INTERPRET = False


def local_backward(inputs, upstream, gain_qk, gain_value):
    rows, width = inputs.shape
    heads = width // HEAD_DIM
    count = rows // SEQ_LEN
    tile = pl.BlockSpec((SEQ_LEN, HEAD_DIM), lambda h, n: (n, h))
    gain = pl.BlockSpec((1, HEAD_DIM), lambda h, n: (0, h))
    flops = heads * count * 5 * 2 * SEQ_LEN * SEQ_LEN * HEAD_DIM
    grad_in, qk_part, value_part = pl.pallas_call(
        attention_kernel,
        grid=(heads, count),
        in_specs=[tile, tile, gain, gain],
        out_specs=[tile, gain, gain],
        out_shape=[
            jax.ShapeDtypeStruct((rows, width), jnp.bfloat16),
            jax.ShapeDtypeStruct((1, width), jnp.float32),
            jax.ShapeDtypeStruct((1, width), jnp.float32),
        ],
        cost_estimate=pl.CostEstimate(
            flops=flops,
            transcendentals=heads * count * SEQ_LEN * SEQ_LEN,
            bytes_accessed=3 * rows * width * 2,
        ),
        interpret=INTERPRET,
    )(inputs, upstream, gain_qk[None], gain_value[None])
    return grad_in, qk_part[0], value_part[0]


def to_heads(block):
    return lax.all_to_all(block, "tp", split_axis=block.ndim - 1, concat_axis=block.ndim - 2, tiled=True)


def shards(saved_inputs, incoming, qk_gain, value_gain):
    tick_count = saved_inputs.shape[0]
    local_width = qk_gain.shape[1] // lax.axis_size("tp")
    offset = lax.axis_index("tp") * local_width
    gain_qk = lax.dynamic_slice_in_dim(qk_gain[0], offset, local_width)
    gain_value = lax.dynamic_slice_in_dim(value_gain[0], offset, local_width)
    first = to_heads(jnp.stack([saved_inputs[0, 0], incoming[0]]))
    inputs_heads = [first[0]]
    for t in range(1, tick_count):
        first, later = lax.optimization_barrier((first, saved_inputs[t, 0]))
        inputs_heads.append(to_heads(later))
    upstream = first[1]
    qk_sum = jnp.zeros((local_width,), jnp.float32)
    value_sum = jnp.zeros((local_width,), jnp.float32)
    for tick_index in range(tick_count):
        grad_in, qk_part, value_part = local_backward(
            inputs_heads[tick_index], upstream, gain_qk, gain_value
        )
        qk_sum = qk_sum + qk_part
        value_sum = value_sum + value_part
        upstream = pass_on(grad_in)
    passed = lax.all_to_all(upstream, "tp", split_axis=0, concat_axis=1, tiled=True)
    return (passed[None], qk_sum[None], value_sum[None])


def solution(mesh):
    return jax.shard_map(
        shards,
        mesh=mesh,
        in_specs=(
            P(None, "section", "tp", None),
            P("section", "tp", None),
            P("section", None),
            P("section", None),
        ),
        out_specs=(P("section", "tp", None), P("section", "tp"), P("section", "tp")),
        check_vma=False,
    )
```

```python
import jax
import jax.numpy as jnp
from jax import lax
from jax.sharding import PartitionSpec as P
from jax.experimental import pallas as pl

HEAD_DIM = 128
SEQ_LEN = 256


def from_behind(block, axis, distance):
    devices = range(lax.axis_size(axis))
    route = [((i - distance) % len(devices), i) for i in devices]
    return lax.ppermute(block, axis, route)


def pass_on(grad_in):
    return from_behind(grad_in, "section", -1)


def attention_kernel(x_ref, u_ref, gq_ref, gv_ref, g_ref, qs_ref, vs_ref):
    n = pl.program_id(1)
    scale = HEAD_DIM ** (-0.5)
    wide = x_ref[...].astype(jnp.float32)
    gq = gq_ref[...]
    gv = gv_ref[...]
    keys = (wide * gq).astype(jnp.bfloat16)
    values = (wide * gv).astype(jnp.bfloat16)
    up = u_ref[...]
    nt = (((1,), (1,)), ((), ()))
    tn = (((0,), (0,)), ((), ()))
    scores = lax.dot_general(keys, keys, nt, preferred_element_type=jnp.float32) * scale
    rows = lax.broadcasted_iota(jnp.int32, scores.shape, 0)
    cols = lax.broadcasted_iota(jnp.int32, scores.shape, 1)
    scores = jnp.where(cols <= rows, scores, -jnp.inf)
    row_max = jnp.max(scores, axis=1, keepdims=True)
    weights = jnp.exp(scores - row_max)
    probs = weights / jnp.sum(weights, axis=1, keepdims=True)
    prob_grad = lax.dot_general(up, values, nt, preferred_element_type=jnp.float32)
    score_grad = probs * (prob_grad - jnp.sum(probs * prob_grad, axis=1, keepdims=True))
    score_low = score_grad.astype(jnp.bfloat16)
    probs_low = probs.astype(jnp.bfloat16)
    query_grad = jnp.dot(score_low, keys, preferred_element_type=jnp.float32) * scale
    key_grad = lax.dot_general(score_low, keys, tn, preferred_element_type=jnp.float32) * scale
    value_grad = lax.dot_general(probs_low, up, tn, preferred_element_type=jnp.float32)
    qk_total = query_grad + key_grad
    g_ref[...] = (up.astype(jnp.float32) + qk_total * gq + value_grad * gv).astype(jnp.bfloat16)
    qk_part = jnp.sum(wide * qk_total, axis=0, keepdims=True)
    value_part = jnp.sum(wide * value_grad, axis=0, keepdims=True)

    @pl.when(n == 0)
    def _():
        qs_ref[...] = qk_part
        vs_ref[...] = value_part

    @pl.when(n > 0)
    def _():
        qs_ref[...] += qk_part
        vs_ref[...] += value_part


INTERPRET = False


def local_backward(inputs, upstream, gain_qk, gain_value):
    rows, width = inputs.shape
    heads = width // HEAD_DIM
    count = rows // SEQ_LEN
    tile = pl.BlockSpec((SEQ_LEN, HEAD_DIM), lambda h, n: (n, h))
    gain = pl.BlockSpec((1, HEAD_DIM), lambda h, n: (0, h))
    flops = heads * count * 5 * 2 * SEQ_LEN * SEQ_LEN * HEAD_DIM
    grad_in, qk_part, value_part = pl.pallas_call(
        attention_kernel,
        grid=(heads, count),
        in_specs=[tile, tile, gain, gain],
        out_specs=[tile, gain, gain],
        out_shape=[
            jax.ShapeDtypeStruct((rows, width), jnp.bfloat16),
            jax.ShapeDtypeStruct((1, width), jnp.float32),
            jax.ShapeDtypeStruct((1, width), jnp.float32),
        ],
        cost_estimate=pl.CostEstimate(
            flops=flops,
            transcendentals=heads * count * SEQ_LEN * SEQ_LEN,
            bytes_accessed=3 * rows * width * 2,
        ),
        interpret=INTERPRET,
    )(inputs, upstream, gain_qk[None], gain_value[None])
    return grad_in, qk_part[0], value_part[0]


def to_heads(block):
    return lax.all_to_all(block, "tp", split_axis=block.ndim - 1, concat_axis=block.ndim - 2, tiled=True)


def shards(saved_inputs, incoming, qk_gain, value_gain):
    local_width = qk_gain.shape[1] // lax.axis_size("tp")
    offset = lax.axis_index("tp") * local_width
    gain_qk = lax.dynamic_slice_in_dim(qk_gain[0], offset, local_width)
    gain_value = lax.dynamic_slice_in_dim(value_gain[0], offset, local_width)
    gains_next = pass_on(jnp.stack([gain_qk, gain_value]))
    inputs_next = pass_on(saved_inputs[1, 0])
    first = to_heads(jnp.stack([saved_inputs[0, 0], incoming[0]]))
    grad_0, qk_0, value_0 = local_backward(first[0], first[1], gain_qk, gain_value)
    upstream_next = from_behind(grad_0, "section", -2)
    first, later = lax.optimization_barrier((first, inputs_next))
    inputs_heads = to_heads(later)
    grad_1, qk_1, value_1 = local_backward(inputs_heads, upstream_next, gains_next[0], gains_next[1])
    sums_1 = from_behind(jnp.stack([qk_1, value_1]), "section", 1)
    passed = lax.all_to_all(grad_1, "tp", split_axis=0, concat_axis=1, tiled=True)
    return (passed[None], (qk_0 + sums_1[0])[None], (value_0 + sums_1[1])[None])


def solution(mesh):
    return jax.shard_map(
        shards,
        mesh=mesh,
        in_specs=(
            P(None, "section", "tp", None),
            P("section", "tp", None),
            P("section", None),
            P("section", None),
        ),
        out_specs=(P("section", "tp", None), P("section", "tp"), P("section", "tp")),
        check_vma=False,
    )
```

```python
import jax
import jax.numpy as jnp
from jax import lax
from jax.sharding import PartitionSpec as P
from jax.experimental import pallas as pl

HEAD_DIM = 128
SEQ_LEN = 256


def from_behind(block, axis, distance):
    devices = range(lax.axis_size(axis))
    route = [((i - distance) % len(devices), i) for i in devices]
    return lax.ppermute(block, axis, route)


def pass_on(grad_in):
    return from_behind(grad_in, "section", -1)


def attention_kernel(x_ref, u_ref, gq_ref, gv_ref, g_ref, qs_ref, vs_ref):
    n = pl.program_id(1)
    scale = HEAD_DIM ** (-0.5)
    wide = x_ref[...].astype(jnp.float32)
    gq = gq_ref[...]
    gv = gv_ref[...]
    keys = (wide * gq).astype(jnp.bfloat16)
    values = (wide * gv).astype(jnp.bfloat16)
    up = u_ref[...]
    nt = (((1,), (1,)), ((), ()))
    tn = (((0,), (0,)), ((), ()))
    scores = lax.dot_general(keys, keys, nt, preferred_element_type=jnp.float32) * scale
    rows = lax.broadcasted_iota(jnp.int32, scores.shape, 0)
    cols = lax.broadcasted_iota(jnp.int32, scores.shape, 1)
    scores = jnp.where(cols <= rows, scores, -jnp.inf)
    row_max = jnp.max(scores, axis=1, keepdims=True)
    weights = jnp.exp(scores - row_max)
    probs = weights / jnp.sum(weights, axis=1, keepdims=True)
    prob_grad = lax.dot_general(up, values, nt, preferred_element_type=jnp.float32)
    score_grad = probs * (prob_grad - jnp.sum(probs * prob_grad, axis=1, keepdims=True))
    score_low = score_grad.astype(jnp.bfloat16)
    probs_low = probs.astype(jnp.bfloat16)
    query_grad = jnp.dot(score_low, keys, preferred_element_type=jnp.float32) * scale
    key_grad = lax.dot_general(score_low, keys, tn, preferred_element_type=jnp.float32) * scale
    value_grad = lax.dot_general(probs_low, up, tn, preferred_element_type=jnp.float32)
    qk_total = query_grad + key_grad
    g_ref[...] = (up.astype(jnp.float32) + qk_total * gq + value_grad * gv).astype(jnp.bfloat16)
    qk_part = jnp.sum(wide * qk_total, axis=0, keepdims=True)
    value_part = jnp.sum(wide * value_grad, axis=0, keepdims=True)

    @pl.when(n == 0)
    def _():
        qs_ref[...] = qk_part
        vs_ref[...] = value_part

    @pl.when(n > 0)
    def _():
        qs_ref[...] += qk_part
        vs_ref[...] += value_part


INTERPRET = False


def local_backward(inputs, upstream, gain_qk, gain_value):
    rows, width = inputs.shape
    heads = width // HEAD_DIM
    count = rows // SEQ_LEN
    tile = pl.BlockSpec((SEQ_LEN, HEAD_DIM), lambda h, n: (n, h))
    gain = pl.BlockSpec((1, HEAD_DIM), lambda h, n: (0, h))
    flops = heads * count * 5 * 2 * SEQ_LEN * SEQ_LEN * HEAD_DIM
    grad_in, qk_part, value_part = pl.pallas_call(
        attention_kernel,
        grid=(heads, count),
        in_specs=[tile, tile, gain, gain],
        out_specs=[tile, gain, gain],
        out_shape=[
            jax.ShapeDtypeStruct((rows, width), jnp.bfloat16),
            jax.ShapeDtypeStruct((1, width), jnp.float32),
            jax.ShapeDtypeStruct((1, width), jnp.float32),
        ],
        cost_estimate=pl.CostEstimate(
            flops=flops,
            transcendentals=heads * count * SEQ_LEN * SEQ_LEN,
            bytes_accessed=3 * rows * width * 2,
        ),
        interpret=INTERPRET,
    )(inputs, upstream, gain_qk[None], gain_value[None])
    return grad_in, qk_part[0], value_part[0]


def to_heads(block):
    return lax.all_to_all(block, "tp", split_axis=block.ndim - 1, concat_axis=block.ndim - 2, tiled=True)


def shards(saved_inputs, incoming, qk_gain, value_gain):
    local_width = qk_gain.shape[1] // lax.axis_size("tp")
    offset = lax.axis_index("tp") * local_width
    gain_qk = lax.dynamic_slice_in_dim(qk_gain[0], offset, local_width)
    gain_value = lax.dynamic_slice_in_dim(value_gain[0], offset, local_width)
    gains_next = pass_on(jnp.stack([gain_qk, gain_value]))
    inputs_next = pass_on(saved_inputs[1, 0])
    first = to_heads(jnp.stack([saved_inputs[0, 0], incoming[0]]))
    first, gains_next = lax.optimization_barrier((first, gains_next))
    grad_0, qk_0, value_0 = local_backward(first[0], first[1], gain_qk, gain_value)
    upstream_next = from_behind(grad_0, "section", -2)
    first, later = lax.optimization_barrier((first, inputs_next))
    inputs_heads = to_heads(later)
    grad_1, qk_1, value_1 = local_backward(inputs_heads, upstream_next, gains_next[0], gains_next[1])
    sums_1 = from_behind(jnp.stack([qk_1, value_1]), "section", 1)
    passed = lax.all_to_all(grad_1, "tp", split_axis=0, concat_axis=1, tiled=True)
    return (passed[None], (qk_0 + sums_1[0])[None], (value_0 + sums_1[1])[None])


def solution(mesh):
    return jax.shard_map(
        shards,
        mesh=mesh,
        in_specs=(
            P(None, "section", "tp", None),
            P("section", "tp", None),
            P("section", None),
            P("section", None),
        ),
        out_specs=(P("section", "tp", None), P("section", "tp"), P("section", "tp")),
        check_vma=False,
    )
```

```python
import jax
import jax.numpy as jnp
from jax import lax
from jax.sharding import PartitionSpec as P
from jax.experimental import pallas as pl

HEAD_DIM = 128
SEQ_LEN = 256


def from_behind(block, axis, distance):
    devices = range(lax.axis_size(axis))
    route = [((i - distance) % len(devices), i) for i in devices]
    return lax.ppermute(block, axis, route)


def pass_on(grad_in):
    return from_behind(grad_in, "section", -1)


def attention_kernel(x_ref, u_ref, gq_ref, gv_ref, g_ref, qs_ref, vs_ref):
    n = pl.program_id(1)
    scale = HEAD_DIM ** (-0.5)
    wide = x_ref[...].reshape(SEQ_LEN, HEAD_DIM).astype(jnp.float32)
    gq = gq_ref[...]
    gv = gv_ref[...]
    keys = (wide * gq).astype(jnp.bfloat16)
    values = (wide * gv).astype(jnp.bfloat16)
    up = u_ref[...].reshape(SEQ_LEN, HEAD_DIM)
    nt = (((1,), (1,)), ((), ()))
    tn = (((0,), (0,)), ((), ()))
    scores = lax.dot_general(keys, keys, nt, preferred_element_type=jnp.float32) * scale
    rows = lax.broadcasted_iota(jnp.int32, scores.shape, 0)
    cols = lax.broadcasted_iota(jnp.int32, scores.shape, 1)
    scores = jnp.where(cols <= rows, scores, -jnp.inf)
    row_max = jnp.max(scores, axis=1, keepdims=True)
    weights = jnp.exp(scores - row_max)
    probs = weights / jnp.sum(weights, axis=1, keepdims=True)
    prob_grad = lax.dot_general(up, values, nt, preferred_element_type=jnp.float32)
    score_grad = probs * (prob_grad - jnp.sum(probs * prob_grad, axis=1, keepdims=True))
    score_low = score_grad.astype(jnp.bfloat16)
    probs_low = probs.astype(jnp.bfloat16)
    query_grad = jnp.dot(score_low, keys, preferred_element_type=jnp.float32) * scale
    key_grad = lax.dot_general(score_low, keys, tn, preferred_element_type=jnp.float32) * scale
    value_grad = lax.dot_general(probs_low, up, tn, preferred_element_type=jnp.float32)
    qk_total = query_grad + key_grad
    grad_in = (up.astype(jnp.float32) + qk_total * gq + value_grad * gv).astype(jnp.bfloat16)
    g_ref[...] = grad_in.reshape(g_ref.shape)
    qk_part = jnp.sum(wide * qk_total, axis=0, keepdims=True)
    value_part = jnp.sum(wide * value_grad, axis=0, keepdims=True)

    @pl.when(n == 0)
    def _():
        qs_ref[...] = qk_part
        vs_ref[...] = value_part

    @pl.when(n > 0)
    def _():
        qs_ref[...] += qk_part
        vs_ref[...] += value_part


INTERPRET = False


def tile_of(array, slot):
    half = array.shape[-2]
    if slot is None:
        return pl.BlockSpec((2, half, HEAD_DIM), lambda h, n: (n, 0, h))
    return pl.BlockSpec((2, None, half, HEAD_DIM), lambda h, n: (n, slot, 0, h))


def local_backward(inputs, inputs_slot, upstream, upstream_slot, gain_qk, gain_value):
    blocks, half, width = upstream.shape[0], upstream.shape[-2], upstream.shape[-1]
    heads = width // HEAD_DIM
    count = blocks * half // SEQ_LEN
    gain = pl.BlockSpec((1, HEAD_DIM), lambda h, n: (0, h))
    flops = heads * count * 5 * 2 * SEQ_LEN * SEQ_LEN * HEAD_DIM
    grad_in, qk_part, value_part = pl.pallas_call(
        attention_kernel,
        grid=(heads, count),
        in_specs=[tile_of(inputs, inputs_slot), tile_of(upstream, upstream_slot), gain, gain],
        out_specs=[tile_of(upstream, None), gain, gain],
        out_shape=[
            jax.ShapeDtypeStruct((blocks, half, width), jnp.bfloat16),
            jax.ShapeDtypeStruct((1, width), jnp.float32),
            jax.ShapeDtypeStruct((1, width), jnp.float32),
        ],
        cost_estimate=pl.CostEstimate(
            flops=flops,
            transcendentals=heads * count * SEQ_LEN * SEQ_LEN,
            bytes_accessed=3 * blocks * half * width * 2,
        ),
        interpret=INTERPRET,
    )(inputs, upstream, gain_qk[None], gain_value[None])
    return grad_in, qk_part[0], value_part[0]


def to_heads(block):
    parts = lax.axis_size("tp")
    lead = block.shape[:-2]
    split = block.reshape(lead + (block.shape[-2], parts, block.shape[-1] // parts))
    order = (len(lead) + 1,) + tuple(range(len(lead))) + (len(lead), len(lead) + 2)
    return lax.all_to_all(jnp.transpose(split, order), "tp", 0, 0, tiled=True)


def to_tokens(block):
    back = lax.all_to_all(block, "tp", 0, 0, tiled=True)
    return jnp.transpose(back, (1, 0, 2)).reshape(block.shape[1], -1)


def shards(saved_inputs, incoming, qk_gain, value_gain):
    tick_count = saved_inputs.shape[0]
    local_width = qk_gain.shape[1] // lax.axis_size("tp")
    offset = lax.axis_index("tp") * local_width
    gain_qk = lax.dynamic_slice_in_dim(qk_gain[0], offset, local_width)
    gain_value = lax.dynamic_slice_in_dim(value_gain[0], offset, local_width)
    first = to_heads(jnp.stack([saved_inputs[0, 0], incoming[0]]))
    grad_in, qk_sum, value_sum = local_backward(first, 0, first, 1, gain_qk, gain_value)
    for t in range(1, tick_count):
        first, later = lax.optimization_barrier((first, saved_inputs[t, 0]))
        inputs_heads = to_heads(later)
        upstream = pass_on(grad_in)
        grad_in, qk_part, value_part = local_backward(
            inputs_heads, None, upstream, None, gain_qk, gain_value
        )
        qk_sum = qk_sum + qk_part
        value_sum = value_sum + value_part
    passed = to_tokens(pass_on(grad_in))
    return (passed[None], qk_sum[None], value_sum[None])


def solution(mesh):
    return jax.shard_map(
        shards,
        mesh=mesh,
        in_specs=(
            P(None, "section", "tp", None),
            P("section", "tp", None),
            P("section", None),
            P("section", None),
        ),
        out_specs=(P("section", "tp", None), P("section", "tp"), P("section", "tp")),
        check_vma=False,
    )
```

```python
import jax
import jax.numpy as jnp
from jax import lax
from jax.sharding import PartitionSpec as P
from jax.experimental import pallas as pl

HEAD_DIM = 128
SEQ_LEN = 256


def from_behind(block, axis, distance):
    devices = range(lax.axis_size(axis))
    route = [((i - distance) % len(devices), i) for i in devices]
    return lax.ppermute(block, axis, route)


def pass_on(grad_in):
    return from_behind(grad_in, "section", -1)


def attention_kernel(x_ref, u_ref, gq_ref, gv_ref, g_ref, qs_ref, vs_ref):
    n = pl.program_id(1)
    scale = HEAD_DIM ** (-0.5)
    wide = x_ref[...].reshape(SEQ_LEN, HEAD_DIM).astype(jnp.float32)
    gq = gq_ref[...]
    gv = gv_ref[...]
    keys = (wide * gq).astype(jnp.bfloat16)
    values = (wide * gv).astype(jnp.bfloat16)
    up = u_ref[...].reshape(SEQ_LEN, HEAD_DIM)
    nt = (((1,), (1,)), ((), ()))
    tn = (((0,), (0,)), ((), ()))
    scores = lax.dot_general(keys, keys, nt, preferred_element_type=jnp.float32) * scale
    rows = lax.broadcasted_iota(jnp.int32, scores.shape, 0)
    cols = lax.broadcasted_iota(jnp.int32, scores.shape, 1)
    scores = jnp.where(cols <= rows, scores, -jnp.inf)
    row_max = jnp.max(scores, axis=1, keepdims=True)
    weights = jnp.exp(scores - row_max)
    probs = weights / jnp.sum(weights, axis=1, keepdims=True)
    prob_grad = lax.dot_general(up, values, nt, preferred_element_type=jnp.float32)
    score_grad = probs * (prob_grad - jnp.sum(probs * prob_grad, axis=1, keepdims=True))
    score_low = score_grad.astype(jnp.bfloat16)
    probs_low = probs.astype(jnp.bfloat16)
    query_grad = jnp.dot(score_low, keys, preferred_element_type=jnp.float32) * scale
    key_grad = lax.dot_general(score_low, keys, tn, preferred_element_type=jnp.float32) * scale
    value_grad = lax.dot_general(probs_low, up, tn, preferred_element_type=jnp.float32)
    qk_total = query_grad + key_grad
    grad_in = (up.astype(jnp.float32) + qk_total * gq + value_grad * gv).astype(jnp.bfloat16)
    g_ref[...] = grad_in.reshape(g_ref.shape)
    qk_part = jnp.sum(wide * qk_total, axis=0, keepdims=True)
    value_part = jnp.sum(wide * value_grad, axis=0, keepdims=True)

    @pl.when(n == 0)
    def _():
        qs_ref[...] = qk_part
        vs_ref[...] = value_part

    @pl.when(n > 0)
    def _():
        qs_ref[...] += qk_part
        vs_ref[...] += value_part


INTERPRET = False


def tile_of(array, slot):
    half = array.shape[-2]
    if slot is None:
        return pl.BlockSpec((2, half, HEAD_DIM), lambda h, n: (n, 0, h))
    return pl.BlockSpec((2, None, half, HEAD_DIM), lambda h, n: (n, slot, 0, h))


def local_backward(inputs, inputs_slot, upstream, upstream_slot, gain_qk, gain_value):
    blocks, half, width = upstream.shape[0], upstream.shape[-2], upstream.shape[-1]
    heads = width // HEAD_DIM
    count = blocks * half // SEQ_LEN
    gain = pl.BlockSpec((1, HEAD_DIM), lambda h, n: (0, h))
    flops = heads * count * 5 * 2 * SEQ_LEN * SEQ_LEN * HEAD_DIM
    grad_in, qk_part, value_part = pl.pallas_call(
        attention_kernel,
        grid=(heads, count),
        in_specs=[tile_of(inputs, inputs_slot), tile_of(upstream, upstream_slot), gain, gain],
        out_specs=[tile_of(upstream, None), gain, gain],
        out_shape=[
            jax.ShapeDtypeStruct((blocks, half, width), jnp.bfloat16),
            jax.ShapeDtypeStruct((1, width), jnp.float32),
            jax.ShapeDtypeStruct((1, width), jnp.float32),
        ],
        cost_estimate=pl.CostEstimate(
            flops=flops,
            transcendentals=heads * count * SEQ_LEN * SEQ_LEN,
            bytes_accessed=3 * blocks * half * width * 2,
        ),
        interpret=INTERPRET,
    )(inputs, upstream, gain_qk[None], gain_value[None])
    return grad_in, qk_part[0], value_part[0]


def split_kernel(a_ref, b_ref, c_ref, first_ref, later_ref):
    first_ref[0, 0] = a_ref[...]
    first_ref[0, 1] = b_ref[...]
    later_ref[0] = c_ref[...]


def split_blocks(saved_inputs, incoming):
    parts = lax.axis_size("tp")
    ticks, _, rows, width = saved_inputs.shape
    cut = width // parts
    stacked = saved_inputs.reshape(ticks, rows, width)
    grad = incoming.reshape(rows, width)
    return pl.pallas_call(
        split_kernel,
        grid=(parts,),
        in_specs=[
            pl.BlockSpec((None, rows, cut), lambda j: (0, 0, j)),
            pl.BlockSpec((rows, cut), lambda j: (0, j)),
            pl.BlockSpec((None, rows, cut), lambda j: (1, 0, j)),
        ],
        out_specs=[
            pl.BlockSpec((1, 2, rows, cut), lambda j: (j, 0, 0, 0)),
            pl.BlockSpec((1, rows, cut), lambda j: (j, 0, 0)),
        ],
        out_shape=[
            jax.ShapeDtypeStruct((parts, 2, rows, cut), saved_inputs.dtype),
            jax.ShapeDtypeStruct((parts, rows, cut), saved_inputs.dtype),
        ],
        interpret=INTERPRET,
    )(stacked, grad, stacked)


def to_heads(block):
    return lax.all_to_all(block, "tp", 0, 0, tiled=True)


def to_tokens(block):
    back = lax.all_to_all(block, "tp", 0, 0, tiled=True)
    return jnp.transpose(back, (1, 0, 2)).reshape(block.shape[1], -1)


def shards(saved_inputs, incoming, qk_gain, value_gain):
    tick_count = saved_inputs.shape[0]
    local_width = qk_gain.shape[1] // lax.axis_size("tp")
    offset = lax.axis_index("tp") * local_width
    gain_qk = lax.dynamic_slice_in_dim(qk_gain[0], offset, local_width)
    gain_value = lax.dynamic_slice_in_dim(value_gain[0], offset, local_width)
    first, later = split_blocks(saved_inputs, incoming)
    first = to_heads(first)
    grad_in, qk_sum, value_sum = local_backward(first, 0, first, 1, gain_qk, gain_value)
    for t in range(1, tick_count):
        first, later = lax.optimization_barrier((first, later))
        inputs_heads = to_heads(later)
        upstream = pass_on(grad_in)
        grad_in, qk_part, value_part = local_backward(
            inputs_heads, None, upstream, None, gain_qk, gain_value
        )
        qk_sum = qk_sum + qk_part
        value_sum = value_sum + value_part
    passed = to_tokens(pass_on(grad_in))
    return (passed[None], qk_sum[None], value_sum[None])


def solution(mesh):
    return jax.shard_map(
        shards,
        mesh=mesh,
        in_specs=(
            P(None, "section", "tp", None),
            P("section", "tp", None),
            P("section", None),
            P("section", None),
        ),
        out_specs=(P("section", "tp", None), P("section", "tp"), P("section", "tp")),
        check_vma=False,
    )
```

```python
import jax
import jax.numpy as jnp
from jax import lax
from jax.sharding import PartitionSpec as P
from jax.experimental import pallas as pl
from jax.experimental.pallas import tpu as pltpu

HEAD_DIM = 128
SEQ_LEN = 256


def from_behind(block, axis, distance):
    devices = range(lax.axis_size(axis))
    route = [((i - distance) % len(devices), i) for i in devices]
    return lax.ppermute(block, axis, route)


def pass_on(grad_in):
    return from_behind(grad_in, "section", -1)


def attend_head(wide, up, gq, gv):
    scale = HEAD_DIM ** (-0.5)
    keys = (wide * gq).astype(jnp.bfloat16)
    values = (wide * gv).astype(jnp.bfloat16)
    nt = (((1,), (1,)), ((), ()))
    tn = (((0,), (0,)), ((), ()))
    scores = lax.dot_general(keys, keys, nt, preferred_element_type=jnp.float32) * scale
    rows = lax.broadcasted_iota(jnp.int32, scores.shape, 0)
    cols = lax.broadcasted_iota(jnp.int32, scores.shape, 1)
    scores = jnp.where(cols <= rows, scores, -jnp.inf)
    row_max = jnp.max(scores, axis=1, keepdims=True)
    weights = jnp.exp(scores - row_max)
    probs = weights / jnp.sum(weights, axis=1, keepdims=True)
    prob_grad = lax.dot_general(up, values, nt, preferred_element_type=jnp.float32)
    score_grad = probs * (prob_grad - jnp.sum(probs * prob_grad, axis=1, keepdims=True))
    score_low = score_grad.astype(jnp.bfloat16)
    probs_low = probs.astype(jnp.bfloat16)
    query_grad = jnp.dot(score_low, keys, preferred_element_type=jnp.float32) * scale
    key_grad = lax.dot_general(score_low, keys, tn, preferred_element_type=jnp.float32) * scale
    value_grad = lax.dot_general(probs_low, up, tn, preferred_element_type=jnp.float32)
    qk_total = query_grad + key_grad
    grad_in = (up.astype(jnp.float32) + qk_total * gq + value_grad * gv).astype(jnp.bfloat16)
    qk_part = jnp.sum(wide * qk_total, axis=0, keepdims=True)
    value_part = jnp.sum(wide * value_grad, axis=0, keepdims=True)
    return grad_in, qk_part, value_part


def attention_kernel(x_ref, u_ref, gq_ref, gv_ref, g_ref, qs_ref, vs_ref):
    n = pl.program_id(0)
    heads = g_ref.shape[-1] // HEAD_DIM
    for h in range(heads):
        cols = slice(h * HEAD_DIM, (h + 1) * HEAD_DIM)
        wide = x_ref[:, :, cols].reshape(SEQ_LEN, HEAD_DIM).astype(jnp.float32)
        up = u_ref[:, :, cols].reshape(SEQ_LEN, HEAD_DIM)
        grad_in, qk_part, value_part = attend_head(wide, up, gq_ref[:, cols], gv_ref[:, cols])
        g_ref[:, :, cols] = grad_in.reshape(g_ref.shape[0], g_ref.shape[1], HEAD_DIM)

        @pl.when(n == 0)
        def _():
            qs_ref[:, cols] = qk_part
            vs_ref[:, cols] = value_part

        @pl.when(n > 0)
        def _():
            qs_ref[:, cols] += qk_part
            vs_ref[:, cols] += value_part


INTERPRET = False


def tile_of(array, slot):
    half, width = array.shape[-2], array.shape[-1]
    if slot is None:
        return pl.BlockSpec((2, half, width), lambda n: (n, 0, 0))
    return pl.BlockSpec((2, None, half, width), lambda n: (n, slot, 0, 0))


def local_backward(inputs, inputs_slot, upstream, upstream_slot, gain_qk, gain_value):
    blocks, half, width = upstream.shape[0], upstream.shape[-2], upstream.shape[-1]
    heads = width // HEAD_DIM
    count = blocks * half // SEQ_LEN
    gain = pl.BlockSpec((1, width), lambda n: (0, 0))
    flops = heads * count * 5 * 2 * SEQ_LEN * SEQ_LEN * HEAD_DIM
    grad_in, qk_part, value_part = pl.pallas_call(
        attention_kernel,
        grid=(count,),
        in_specs=[tile_of(inputs, inputs_slot), tile_of(upstream, upstream_slot), gain, gain],
        out_specs=[tile_of(upstream, None), gain, gain],
        out_shape=[
            jax.ShapeDtypeStruct((blocks, half, width), jnp.bfloat16),
            jax.ShapeDtypeStruct((1, width), jnp.float32),
            jax.ShapeDtypeStruct((1, width), jnp.float32),
        ],
        cost_estimate=pl.CostEstimate(
            flops=flops,
            transcendentals=heads * count * SEQ_LEN * SEQ_LEN,
            bytes_accessed=3 * blocks * half * width * 2,
        ),
        interpret=INTERPRET,
    )(inputs, upstream, gain_qk[None], gain_value[None])
    return grad_in, qk_part[0], value_part[0]


def split_blocks(saved_inputs, incoming):
    parts = lax.axis_size("tp")
    ticks, _, rows, width = saved_inputs.shape
    cut = width // parts
    stacked = saved_inputs.reshape(ticks, rows, width)
    grad = incoming.reshape(rows, width)

    def split_kernel(x_hbm, g_hbm, first_hbm, later_hbm, sems):
        copies = []
        for j in range(parts):
            cols = pl.ds(j * cut, cut)
            copies.append(pltpu.make_async_copy(x_hbm.at[0, :, cols], first_hbm.at[j, 0], sems.at[0, j]))
            copies.append(pltpu.make_async_copy(g_hbm.at[:, cols], first_hbm.at[j, 1], sems.at[1, j]))
            copies.append(pltpu.make_async_copy(x_hbm.at[1, :, cols], later_hbm.at[j], sems.at[2, j]))
        for c in copies:
            c.start()
        for c in copies:
            c.wait()

    anywhere = pl.BlockSpec(memory_space=pl.ANY)
    return pl.pallas_call(
        split_kernel,
        in_specs=[anywhere, anywhere],
        out_specs=[anywhere, anywhere],
        out_shape=[
            jax.ShapeDtypeStruct((parts, 2, rows, cut), saved_inputs.dtype),
            jax.ShapeDtypeStruct((parts, rows, cut), saved_inputs.dtype),
        ],
        scratch_shapes=[pltpu.SemaphoreType.DMA((3, parts))],
        interpret=INTERPRET,
    )(stacked, grad)


def to_heads(block):
    return lax.all_to_all(block, "tp", 0, 0, tiled=True)


def to_tokens(block):
    back = lax.all_to_all(block, "tp", 0, 0, tiled=True)
    return jnp.transpose(back, (1, 0, 2)).reshape(block.shape[1], -1)


def shards(saved_inputs, incoming, qk_gain, value_gain):
    tick_count = saved_inputs.shape[0]
    local_width = qk_gain.shape[1] // lax.axis_size("tp")
    offset = lax.axis_index("tp") * local_width
    gain_qk = lax.dynamic_slice_in_dim(qk_gain[0], offset, local_width)
    gain_value = lax.dynamic_slice_in_dim(value_gain[0], offset, local_width)
    first, later = split_blocks(saved_inputs, incoming)
    first = to_heads(first)
    grad_in, qk_sum, value_sum = local_backward(first, 0, first, 1, gain_qk, gain_value)
    for t in range(1, tick_count):
        first, later = lax.optimization_barrier((first, later))
        inputs_heads = to_heads(later)
        upstream = pass_on(grad_in)
        grad_in, qk_part, value_part = local_backward(
            inputs_heads, None, upstream, None, gain_qk, gain_value
        )
        qk_sum = qk_sum + qk_part
        value_sum = value_sum + value_part
    passed = to_tokens(pass_on(grad_in))
    return (passed[None], qk_sum[None], value_sum[None])


def solution(mesh):
    return jax.shard_map(
        shards,
        mesh=mesh,
        in_specs=(
            P(None, "section", "tp", None),
            P("section", "tp", None),
            P("section", None),
            P("section", None),
        ),
        out_specs=(P("section", "tp", None), P("section", "tp"), P("section", "tp")),
        check_vma=False,
    )
```

```python
import jax
import jax.numpy as jnp
from jax import lax
from jax.sharding import PartitionSpec as P
from jax.experimental import pallas as pl

HEAD_DIM = 128
SEQ_LEN = 256


def from_behind(block, axis, distance):
    devices = range(lax.axis_size(axis))
    route = [((i - distance) % len(devices), i) for i in devices]
    return lax.ppermute(block, axis, route)


def pass_on(grad_in):
    return from_behind(grad_in, "section", -1)


def attend_head(wide, up, gq, gv):
    scale = HEAD_DIM ** (-0.5)
    keys = (wide * gq).astype(jnp.bfloat16)
    values = (wide * gv).astype(jnp.bfloat16)
    nt = (((1,), (1,)), ((), ()))
    tn = (((0,), (0,)), ((), ()))
    scores = lax.dot_general(keys, keys, nt, preferred_element_type=jnp.float32) * scale
    rows = lax.broadcasted_iota(jnp.int32, scores.shape, 0)
    cols = lax.broadcasted_iota(jnp.int32, scores.shape, 1)
    scores = jnp.where(cols <= rows, scores, -jnp.inf)
    row_max = jnp.max(scores, axis=1, keepdims=True)
    weights = jnp.exp(scores - row_max)
    probs = weights / jnp.sum(weights, axis=1, keepdims=True)
    prob_grad = lax.dot_general(up, values, nt, preferred_element_type=jnp.float32)
    score_grad = probs * (prob_grad - jnp.sum(probs * prob_grad, axis=1, keepdims=True))
    score_low = score_grad.astype(jnp.bfloat16)
    probs_low = probs.astype(jnp.bfloat16)
    query_grad = jnp.dot(score_low, keys, preferred_element_type=jnp.float32) * scale
    key_grad = lax.dot_general(score_low, keys, tn, preferred_element_type=jnp.float32) * scale
    value_grad = lax.dot_general(probs_low, up, tn, preferred_element_type=jnp.float32)
    qk_total = query_grad + key_grad
    grad_in = (up.astype(jnp.float32) + qk_total * gq + value_grad * gv).astype(jnp.bfloat16)
    qk_part = jnp.sum(wide * qk_total, axis=0, keepdims=True)
    value_part = jnp.sum(wide * value_grad, axis=0, keepdims=True)
    return grad_in, qk_part, value_part


def attention_kernel(x_ref, u_ref, gq_ref, gv_ref, g_ref, qs_ref, vs_ref):
    n = pl.program_id(0)
    heads = g_ref.shape[-1] // HEAD_DIM
    for h in range(heads):
        cols = slice(h * HEAD_DIM, (h + 1) * HEAD_DIM)
        wide = x_ref[:, :, cols].reshape(SEQ_LEN, HEAD_DIM).astype(jnp.float32)
        up = u_ref[:, :, cols].reshape(SEQ_LEN, HEAD_DIM)
        grad_in, qk_part, value_part = attend_head(wide, up, gq_ref[:, cols], gv_ref[:, cols])
        g_ref[:, :, cols] = grad_in.reshape(g_ref.shape[0], g_ref.shape[1], HEAD_DIM)

        @pl.when(n == 0)
        def _():
            qs_ref[:, cols] = qk_part
            vs_ref[:, cols] = value_part

        @pl.when(n > 0)
        def _():
            qs_ref[:, cols] += qk_part
            vs_ref[:, cols] += value_part


INTERPRET = False


def tile_of(array, slot):
    half, width = array.shape[-2], array.shape[-1]
    if slot is None:
        return pl.BlockSpec((2, half, width), lambda n: (n, 0, 0))
    return pl.BlockSpec((2, None, half, width), lambda n: (n, slot, 0, 0))


def local_backward(inputs, inputs_slot, upstream, upstream_slot, gain_qk, gain_value):
    blocks, half, width = upstream.shape[0], upstream.shape[-2], upstream.shape[-1]
    heads = width // HEAD_DIM
    count = blocks * half // SEQ_LEN
    gain = pl.BlockSpec((1, width), lambda n: (0, 0))
    flops = heads * count * 5 * 2 * SEQ_LEN * SEQ_LEN * HEAD_DIM
    grad_in, qk_part, value_part = pl.pallas_call(
        attention_kernel,
        grid=(count,),
        in_specs=[tile_of(inputs, inputs_slot), tile_of(upstream, upstream_slot), gain, gain],
        out_specs=[tile_of(upstream, None), gain, gain],
        out_shape=[
            jax.ShapeDtypeStruct((blocks, half, width), jnp.bfloat16),
            jax.ShapeDtypeStruct((1, width), jnp.float32),
            jax.ShapeDtypeStruct((1, width), jnp.float32),
        ],
        cost_estimate=pl.CostEstimate(
            flops=flops,
            transcendentals=heads * count * SEQ_LEN * SEQ_LEN,
            bytes_accessed=3 * blocks * half * width * 2,
        ),
        interpret=INTERPRET,
    )(inputs, upstream, gain_qk[None], gain_value[None])
    return grad_in, qk_part[0], value_part[0]


def split_blocks(saved_inputs, incoming):
    parts = lax.axis_size("tp")
    ticks, _, rows, width = saved_inputs.shape
    cut = width // parts
    group = 4 if parts % 4 == 0 else 1
    stacked = saved_inputs.reshape(ticks, rows, width)
    grad = incoming.reshape(rows, width)

    def split_kernel(a_ref, b_ref, c_ref, first_ref, later_ref):
        for j in range(group):
            cols = slice(j * cut, (j + 1) * cut)
            first_ref[j, 0] = a_ref[:, cols]
            first_ref[j, 1] = b_ref[:, cols]
            later_ref[j] = c_ref[:, cols]

    return pl.pallas_call(
        split_kernel,
        grid=(parts // group,),
        in_specs=[
            pl.BlockSpec((None, rows, group * cut), lambda j: (0, 0, j)),
            pl.BlockSpec((rows, group * cut), lambda j: (0, j)),
            pl.BlockSpec((None, rows, group * cut), lambda j: (1, 0, j)),
        ],
        out_specs=[
            pl.BlockSpec((group, 2, rows, cut), lambda j: (j, 0, 0, 0)),
            pl.BlockSpec((group, rows, cut), lambda j: (j, 0, 0)),
        ],
        out_shape=[
            jax.ShapeDtypeStruct((parts, 2, rows, cut), saved_inputs.dtype),
            jax.ShapeDtypeStruct((parts, rows, cut), saved_inputs.dtype),
        ],
        interpret=INTERPRET,
    )(stacked, grad, stacked)


def to_heads(block):
    return lax.all_to_all(block, "tp", 0, 0, tiled=True)


def to_tokens(block):
    back = lax.all_to_all(block, "tp", 0, 0, tiled=True)
    return jnp.transpose(back, (1, 0, 2)).reshape(block.shape[1], -1)


def shards(saved_inputs, incoming, qk_gain, value_gain):
    tick_count = saved_inputs.shape[0]
    local_width = qk_gain.shape[1] // lax.axis_size("tp")
    offset = lax.axis_index("tp") * local_width
    gain_qk = lax.dynamic_slice_in_dim(qk_gain[0], offset, local_width)
    gain_value = lax.dynamic_slice_in_dim(value_gain[0], offset, local_width)
    first, later = split_blocks(saved_inputs, incoming)
    first = to_heads(first)
    grad_in, qk_sum, value_sum = local_backward(first, 0, first, 1, gain_qk, gain_value)
    for t in range(1, tick_count):
        first, later = lax.optimization_barrier((first, later))
        inputs_heads = to_heads(later)
        upstream = pass_on(grad_in)
        grad_in, qk_part, value_part = local_backward(
            inputs_heads, None, upstream, None, gain_qk, gain_value
        )
        qk_sum = qk_sum + qk_part
        value_sum = value_sum + value_part
    passed = to_tokens(pass_on(grad_in))
    return (passed[None], qk_sum[None], value_sum[None])


def solution(mesh):
    return jax.shard_map(
        shards,
        mesh=mesh,
        in_specs=(
            P(None, "section", "tp", None),
            P("section", "tp", None),
            P("section", None),
            P("section", None),
        ),
        out_specs=(P("section", "tp", None), P("section", "tp"), P("section", "tp")),
        check_vma=False,
    )
```

```python
import jax
import jax.numpy as jnp
from jax import lax
from jax.sharding import PartitionSpec as P
from jax.experimental import pallas as pl

HEAD_DIM = 128
SEQ_LEN = 256


def from_behind(block, axis, distance):
    devices = range(lax.axis_size(axis))
    route = [((i - distance) % len(devices), i) for i in devices]
    return lax.ppermute(block, axis, route)


def pass_on(grad_in):
    return from_behind(grad_in, "section", -1)


def half_softmax_grads(queries, keys, values, up, offset, scale):
    nt = (((1,), (1,)), ((), ()))
    scores = lax.dot_general(queries, keys, nt, preferred_element_type=jnp.float32) * scale
    rows = lax.broadcasted_iota(jnp.int32, scores.shape, 0) + offset
    cols = lax.broadcasted_iota(jnp.int32, scores.shape, 1)
    scores = jnp.where(cols <= rows, scores, -jnp.inf)
    row_max = jnp.max(scores, axis=1, keepdims=True)
    weights = jnp.exp(scores - row_max)
    probs = weights / jnp.sum(weights, axis=1, keepdims=True)
    prob_grad = lax.dot_general(up, values, nt, preferred_element_type=jnp.float32)
    score_grad = probs * (prob_grad - jnp.sum(probs * prob_grad, axis=1, keepdims=True))
    return probs.astype(jnp.bfloat16), score_grad.astype(jnp.bfloat16)


def attend_head(wide, up, gq, gv):
    scale = HEAD_DIM ** (-0.5)
    half = SEQ_LEN // 2
    keys = (wide * gq).astype(jnp.bfloat16)
    values = (wide * gv).astype(jnp.bfloat16)
    tn = (((0,), (0,)), ((), ()))
    k_a, k_b = keys[:half], keys[half:]
    u_a, u_b = up[:half], up[half:]
    p_a, s_a = half_softmax_grads(k_a, k_a, values[:half], u_a, 0, scale)
    p_b, s_b = half_softmax_grads(k_b, keys, values, u_b, half, scale)
    f32 = jnp.float32
    query_a = jnp.dot(s_a, k_a, preferred_element_type=f32) * scale
    query_b = jnp.dot(s_b, keys, preferred_element_type=f32) * scale
    key_a = (
        lax.dot_general(s_a, k_a, tn, preferred_element_type=f32)
        + lax.dot_general(s_b[:, :half], k_b, tn, preferred_element_type=f32)
    ) * scale
    key_b = lax.dot_general(s_b[:, half:], k_b, tn, preferred_element_type=f32) * scale
    value_a = lax.dot_general(p_a, u_a, tn, preferred_element_type=f32) + lax.dot_general(
        p_b[:, :half], u_b, tn, preferred_element_type=f32
    )
    value_b = lax.dot_general(p_b[:, half:], u_b, tn, preferred_element_type=f32)
    qk_total = jnp.concatenate([query_a + key_a, query_b + key_b], axis=0)
    value_grad = jnp.concatenate([value_a, value_b], axis=0)
    grad_in = (up.astype(f32) + qk_total * gq + value_grad * gv).astype(jnp.bfloat16)
    qk_part = jnp.sum(wide * qk_total, axis=0, keepdims=True)
    value_part = jnp.sum(wide * value_grad, axis=0, keepdims=True)
    return grad_in, qk_part, value_part


def attention_kernel(x_ref, u_ref, gq_ref, gv_ref, g_ref, qs_ref, vs_ref):
    n = pl.program_id(0)
    heads = g_ref.shape[-1] // HEAD_DIM
    for h in range(heads):
        cols = slice(h * HEAD_DIM, (h + 1) * HEAD_DIM)
        wide = x_ref[:, :, cols].reshape(SEQ_LEN, HEAD_DIM).astype(jnp.float32)
        up = u_ref[:, :, cols].reshape(SEQ_LEN, HEAD_DIM)
        grad_in, qk_part, value_part = attend_head(wide, up, gq_ref[:, cols], gv_ref[:, cols])
        g_ref[:, :, cols] = grad_in.reshape(g_ref.shape[0], g_ref.shape[1], HEAD_DIM)

        @pl.when(n == 0)
        def _():
            qs_ref[:, cols] = qk_part
            vs_ref[:, cols] = value_part

        @pl.when(n > 0)
        def _():
            qs_ref[:, cols] += qk_part
            vs_ref[:, cols] += value_part


INTERPRET = False


def tile_of(array, slot):
    half, width = array.shape[-2], array.shape[-1]
    if slot is None:
        return pl.BlockSpec((2, half, width), lambda n: (n, 0, 0))
    return pl.BlockSpec((2, None, half, width), lambda n: (n, slot, 0, 0))


def local_backward(inputs, inputs_slot, upstream, upstream_slot, gain_qk, gain_value):
    blocks, half, width = upstream.shape[0], upstream.shape[-2], upstream.shape[-1]
    heads = width // HEAD_DIM
    count = blocks * half // SEQ_LEN
    gain = pl.BlockSpec((1, width), lambda n: (0, 0))
    flops = heads * count * 5 * 2 * SEQ_LEN * SEQ_LEN * HEAD_DIM
    grad_in, qk_part, value_part = pl.pallas_call(
        attention_kernel,
        grid=(count,),
        in_specs=[tile_of(inputs, inputs_slot), tile_of(upstream, upstream_slot), gain, gain],
        out_specs=[tile_of(upstream, None), gain, gain],
        out_shape=[
            jax.ShapeDtypeStruct((blocks, half, width), jnp.bfloat16),
            jax.ShapeDtypeStruct((1, width), jnp.float32),
            jax.ShapeDtypeStruct((1, width), jnp.float32),
        ],
        cost_estimate=pl.CostEstimate(
            flops=flops,
            transcendentals=heads * count * SEQ_LEN * SEQ_LEN,
            bytes_accessed=3 * blocks * half * width * 2,
        ),
        interpret=INTERPRET,
    )(inputs, upstream, gain_qk[None], gain_value[None])
    return grad_in, qk_part[0], value_part[0]


def split_blocks(saved_inputs, incoming):
    parts = lax.axis_size("tp")
    ticks, _, rows, width = saved_inputs.shape
    cut = width // parts
    group = 4 if parts % 4 == 0 else 1
    stacked = saved_inputs.reshape(ticks, rows, width)
    grad = incoming.reshape(rows, width)

    def split_kernel(a_ref, b_ref, c_ref, first_ref, later_ref):
        for j in range(group):
            cols = slice(j * cut, (j + 1) * cut)
            first_ref[j, 0] = a_ref[:, cols]
            first_ref[j, 1] = b_ref[:, cols]
            later_ref[j] = c_ref[:, cols]

    return pl.pallas_call(
        split_kernel,
        grid=(parts // group,),
        in_specs=[
            pl.BlockSpec((None, rows, group * cut), lambda j: (0, 0, j)),
            pl.BlockSpec((rows, group * cut), lambda j: (0, j)),
            pl.BlockSpec((None, rows, group * cut), lambda j: (1, 0, j)),
        ],
        out_specs=[
            pl.BlockSpec((group, 2, rows, cut), lambda j: (j, 0, 0, 0)),
            pl.BlockSpec((group, rows, cut), lambda j: (j, 0, 0)),
        ],
        out_shape=[
            jax.ShapeDtypeStruct((parts, 2, rows, cut), saved_inputs.dtype),
            jax.ShapeDtypeStruct((parts, rows, cut), saved_inputs.dtype),
        ],
        interpret=INTERPRET,
    )(stacked, grad, stacked)


def to_heads(block):
    return lax.all_to_all(block, "tp", 0, 0, tiled=True)


def to_tokens(block):
    back = lax.all_to_all(block, "tp", 0, 0, tiled=True)
    return jnp.transpose(back, (1, 0, 2)).reshape(block.shape[1], -1)


def shards(saved_inputs, incoming, qk_gain, value_gain):
    tick_count = saved_inputs.shape[0]
    local_width = qk_gain.shape[1] // lax.axis_size("tp")
    offset = lax.axis_index("tp") * local_width
    gain_qk = lax.dynamic_slice_in_dim(qk_gain[0], offset, local_width)
    gain_value = lax.dynamic_slice_in_dim(value_gain[0], offset, local_width)
    first, later = split_blocks(saved_inputs, incoming)
    first, gain_qk, gain_value = lax.optimization_barrier((first, gain_qk, gain_value))
    first = to_heads(first)
    grad_in, qk_sum, value_sum = local_backward(first, 0, first, 1, gain_qk, gain_value)
    for t in range(1, tick_count):
        first, later = lax.optimization_barrier((first, later))
        inputs_heads = to_heads(later)
        upstream = pass_on(grad_in)
        grad_in, qk_part, value_part = local_backward(
            inputs_heads, None, upstream, None, gain_qk, gain_value
        )
        qk_sum = qk_sum + qk_part
        value_sum = value_sum + value_part
    passed = to_tokens(pass_on(grad_in))
    return (passed[None], qk_sum[None], value_sum[None])


def solution(mesh):
    return jax.shard_map(
        shards,
        mesh=mesh,
        in_specs=(
            P(None, "section", "tp", None),
            P("section", "tp", None),
            P("section", None),
            P("section", None),
        ),
        out_specs=(P("section", "tp", None), P("section", "tp"), P("section", "tp")),
        check_vma=False,
    )
```

```python
import jax
import jax.numpy as jnp
from jax import lax
from jax.sharding import PartitionSpec as P
from jax.experimental import pallas as pl

HEAD_DIM = 128
SEQ_LEN = 256


def from_behind(block, axis, distance):
    devices = range(lax.axis_size(axis))
    route = [((i - distance) % len(devices), i) for i in devices]
    return lax.ppermute(block, axis, route)


def pass_on(grad_in):
    return from_behind(grad_in, "section", -1)


def attend_head(wide, up, gq, gv):
    scale = HEAD_DIM ** (-0.5)
    keys = (wide * gq).astype(jnp.bfloat16)
    values = (wide * gv).astype(jnp.bfloat16)
    nt = (((1,), (1,)), ((), ()))
    tn = (((0,), (0,)), ((), ()))
    scores = lax.dot_general(keys, keys, nt, preferred_element_type=jnp.float32) * scale
    rows = lax.broadcasted_iota(jnp.int32, scores.shape, 0)
    cols = lax.broadcasted_iota(jnp.int32, scores.shape, 1)
    scores = jnp.where(cols <= rows, scores, -jnp.inf)
    row_max = jnp.max(scores, axis=1, keepdims=True)
    weights = jnp.exp(scores - row_max)
    probs = weights / jnp.sum(weights, axis=1, keepdims=True)
    prob_grad = lax.dot_general(up, values, nt, preferred_element_type=jnp.float32)
    score_grad = probs * (prob_grad - jnp.sum(probs * prob_grad, axis=1, keepdims=True))
    score_low = score_grad.astype(jnp.bfloat16)
    probs_low = probs.astype(jnp.bfloat16)
    query_grad = jnp.dot(score_low, keys, preferred_element_type=jnp.float32) * scale
    key_grad = lax.dot_general(score_low, keys, tn, preferred_element_type=jnp.float32) * scale
    value_grad = lax.dot_general(probs_low, up, tn, preferred_element_type=jnp.float32)
    qk_total = query_grad + key_grad
    grad_in = (up.astype(jnp.float32) + qk_total * gq + value_grad * gv).astype(jnp.bfloat16)
    qk_part = jnp.sum(wide * qk_total, axis=0, keepdims=True)
    value_part = jnp.sum(wide * value_grad, axis=0, keepdims=True)
    return grad_in, qk_part, value_part


def attention_kernel(x_ref, u_ref, gq_ref, gv_ref, g_ref, qs_ref, vs_ref):
    n = pl.program_id(0)
    heads = g_ref.shape[-1] // HEAD_DIM
    for h in range(heads):
        cols = slice(h * HEAD_DIM, (h + 1) * HEAD_DIM)
        wide = x_ref[:, :, cols].reshape(SEQ_LEN, HEAD_DIM).astype(jnp.float32)
        up = u_ref[:, :, cols].reshape(SEQ_LEN, HEAD_DIM)
        grad_in, qk_part, value_part = attend_head(wide, up, gq_ref[:, cols], gv_ref[:, cols])
        g_ref[:, :, cols] = grad_in.reshape(g_ref.shape[0], g_ref.shape[1], HEAD_DIM)

        @pl.when(n == 0)
        def _():
            qs_ref[:, cols] = qk_part
            vs_ref[:, cols] = value_part

        @pl.when(n > 0)
        def _():
            qs_ref[:, cols] += qk_part
            vs_ref[:, cols] += value_part


INTERPRET = False


def tile_of(array, slot):
    half, width = array.shape[-2], array.shape[-1]
    if slot is None:
        return pl.BlockSpec((2, half, width), lambda n: (n, 0, 0))
    return pl.BlockSpec((2, None, half, width), lambda n: (n, slot, 0, 0))


def local_backward(inputs, inputs_slot, upstream, upstream_slot, gain_qk, gain_value):
    blocks, half, width = upstream.shape[0], upstream.shape[-2], upstream.shape[-1]
    heads = width // HEAD_DIM
    count = blocks * half // SEQ_LEN
    gain = pl.BlockSpec((1, width), lambda n: (0, 0))
    flops = heads * count * 5 * 2 * SEQ_LEN * SEQ_LEN * HEAD_DIM
    grad_in, qk_part, value_part = pl.pallas_call(
        attention_kernel,
        grid=(count,),
        in_specs=[tile_of(inputs, inputs_slot), tile_of(upstream, upstream_slot), gain, gain],
        out_specs=[tile_of(upstream, None), gain, gain],
        out_shape=[
            jax.ShapeDtypeStruct((blocks, half, width), jnp.bfloat16),
            jax.ShapeDtypeStruct((1, width), jnp.float32),
            jax.ShapeDtypeStruct((1, width), jnp.float32),
        ],
        cost_estimate=pl.CostEstimate(
            flops=flops,
            transcendentals=heads * count * SEQ_LEN * SEQ_LEN,
            bytes_accessed=3 * blocks * half * width * 2,
        ),
        interpret=INTERPRET,
    )(inputs, upstream, gain_qk[None], gain_value[None])
    return grad_in, qk_part[0], value_part[0]


def split_blocks(saved_inputs, incoming):
    parts = lax.axis_size("tp")
    ticks, _, rows, width = saved_inputs.shape
    cut = width // parts
    group = 4 if parts % 4 == 0 else 1
    stacked = saved_inputs.reshape(ticks, rows, width)
    grad = incoming.reshape(rows, width)

    def split_kernel(a_ref, b_ref, c_ref, first_ref, later_ref):
        for j in range(group):
            cols = slice(j * cut, (j + 1) * cut)
            first_ref[j, 0] = a_ref[:, cols]
            first_ref[j, 1] = b_ref[:, cols]
            later_ref[j] = c_ref[:, cols]

    return pl.pallas_call(
        split_kernel,
        grid=(parts // group,),
        in_specs=[
            pl.BlockSpec((None, rows, group * cut), lambda j: (0, 0, j)),
            pl.BlockSpec((rows, group * cut), lambda j: (0, j)),
            pl.BlockSpec((None, rows, group * cut), lambda j: (1, 0, j)),
        ],
        out_specs=[
            pl.BlockSpec((group, 2, rows, cut), lambda j: (j, 0, 0, 0)),
            pl.BlockSpec((group, rows, cut), lambda j: (j, 0, 0)),
        ],
        out_shape=[
            jax.ShapeDtypeStruct((parts, 2, rows, cut), saved_inputs.dtype),
            jax.ShapeDtypeStruct((parts, rows, cut), saved_inputs.dtype),
        ],
        interpret=INTERPRET,
    )(stacked, grad, stacked)


def to_heads(block):
    return lax.all_to_all(block, "tp", 0, 0, tiled=True)


def to_tokens(block):
    back = lax.all_to_all(block, "tp", 0, 0, tiled=True)
    return jnp.transpose(back, (1, 0, 2)).reshape(block.shape[1], -1)


def shards(saved_inputs, incoming, qk_gain, value_gain):
    tick_count = saved_inputs.shape[0]
    local_width = qk_gain.shape[1] // lax.axis_size("tp")
    offset = lax.axis_index("tp") * local_width
    gain_qk = lax.dynamic_slice_in_dim(qk_gain[0], offset, local_width)
    gain_value = lax.dynamic_slice_in_dim(value_gain[0], offset, local_width)
    first, later = split_blocks(saved_inputs, incoming)
    first = to_heads(first)
    grad_in, qk_sum, value_sum = local_backward(first, 0, first, 1, gain_qk, gain_value)
    for t in range(1, tick_count):
        first, later = lax.optimization_barrier((first, later))
        inputs_heads = to_heads(later)
        upstream = pass_on(grad_in)
        grad_in, qk_part, value_part = local_backward(
            inputs_heads, None, upstream, None, gain_qk, gain_value
        )
        qk_sum = qk_sum + qk_part
        value_sum = value_sum + value_part
    half = grad_in.shape[1] // 2
    early = to_tokens(pass_on(grad_in[:, :half]))
    late = pass_on(to_tokens(grad_in[:, half:]))
    passed = jnp.concatenate([early, late], axis=0)
    return (passed[None], qk_sum[None], value_sum[None])


def solution(mesh):
    return jax.shard_map(
        shards,
        mesh=mesh,
        in_specs=(
            P(None, "section", "tp", None),
            P("section", "tp", None),
            P("section", None),
            P("section", None),
        ),
        out_specs=(P("section", "tp", None), P("section", "tp"), P("section", "tp")),
        check_vma=False,
    )
```

```python
import jax
import jax.numpy as jnp
from jax import lax
from jax.sharding import PartitionSpec as P
from jax.experimental import pallas as pl

HEAD_DIM = 128
SEQ_LEN = 256


def from_behind(block, axis, distance):
    devices = range(lax.axis_size(axis))
    route = [((i - distance) % len(devices), i) for i in devices]
    return lax.ppermute(block, axis, route)


def pass_on(grad_in):
    return from_behind(grad_in, "section", -1)


def attend_head(wide, up, gq, gv):
    scale = HEAD_DIM ** (-0.5)
    keys = (wide * gq).astype(jnp.bfloat16)
    values = (wide * gv).astype(jnp.bfloat16)
    nt = (((1,), (1,)), ((), ()))
    tn = (((0,), (0,)), ((), ()))
    scores = lax.dot_general(keys, keys, nt, preferred_element_type=jnp.float32) * scale
    rows = lax.broadcasted_iota(jnp.int32, scores.shape, 0)
    cols = lax.broadcasted_iota(jnp.int32, scores.shape, 1)
    scores = jnp.where(cols <= rows, scores, -jnp.inf)
    row_max = jnp.max(scores, axis=1, keepdims=True)
    weights = jnp.exp(scores - row_max)
    probs = weights / jnp.sum(weights, axis=1, keepdims=True)
    prob_grad = lax.dot_general(up, values, nt, preferred_element_type=jnp.float32)
    score_grad = probs * (prob_grad - jnp.sum(probs * prob_grad, axis=1, keepdims=True))
    score_low = score_grad.astype(jnp.bfloat16)
    probs_low = probs.astype(jnp.bfloat16)
    query_grad = jnp.dot(score_low, keys, preferred_element_type=jnp.float32) * scale
    key_grad = lax.dot_general(score_low, keys, tn, preferred_element_type=jnp.float32) * scale
    value_grad = lax.dot_general(probs_low, up, tn, preferred_element_type=jnp.float32)
    qk_total = query_grad + key_grad
    grad_in = (up.astype(jnp.float32) + qk_total * gq + value_grad * gv).astype(jnp.bfloat16)
    qk_part = jnp.sum(wide * qk_total, axis=0, keepdims=True)
    value_part = jnp.sum(wide * value_grad, axis=0, keepdims=True)
    return grad_in, qk_part, value_part


def attention_kernel(x_ref, u_ref, gq_ref, gv_ref, g_ref, qs_ref, vs_ref):
    n = pl.program_id(0)
    heads = g_ref.shape[-1] // HEAD_DIM
    for h in range(heads):
        cols = slice(h * HEAD_DIM, (h + 1) * HEAD_DIM)
        wide = x_ref[:, :, cols].reshape(SEQ_LEN, HEAD_DIM).astype(jnp.float32)
        up = u_ref[:, :, cols].reshape(SEQ_LEN, HEAD_DIM)
        grad_in, qk_part, value_part = attend_head(wide, up, gq_ref[:, cols], gv_ref[:, cols])
        if len(g_ref.shape) == 4:
            parts = grad_in.reshape(g_ref.shape[1], g_ref.shape[0], g_ref.shape[2], HEAD_DIM)
            for r in range(g_ref.shape[0]):
                g_ref[r, :, :, cols] = parts[:, r]
        else:
            g_ref[:, :, cols] = grad_in.reshape(g_ref.shape[0], g_ref.shape[1], HEAD_DIM)

        @pl.when(n == 0)
        def _():
            qs_ref[:, cols] = qk_part
            vs_ref[:, cols] = value_part

        @pl.when(n > 0)
        def _():
            qs_ref[:, cols] += qk_part
            vs_ref[:, cols] += value_part


INTERPRET = False


def tile_of(array, slot):
    half, width = array.shape[-2], array.shape[-1]
    if slot is None:
        return pl.BlockSpec((2, half, width), lambda n: (n, 0, 0))
    return pl.BlockSpec((2, None, half, width), lambda n: (n, slot, 0, 0))


def local_backward(inputs, inputs_slot, upstream, upstream_slot, gain_qk, gain_value, halves=False):
    blocks, half, width = upstream.shape[0], upstream.shape[-2], upstream.shape[-1]
    heads = width // HEAD_DIM
    count = blocks * half // SEQ_LEN
    gain = pl.BlockSpec((1, width), lambda n: (0, 0))
    flops = heads * count * 5 * 2 * SEQ_LEN * SEQ_LEN * HEAD_DIM
    if halves:
        grad_shape = (2, blocks, half // 2, width)
        grad_spec = pl.BlockSpec((2, 2, half // 2, width), lambda n: (0, n, 0, 0))
    else:
        grad_shape = (blocks, half, width)
        grad_spec = tile_of(upstream, None)
    grad_in, qk_part, value_part = pl.pallas_call(
        attention_kernel,
        grid=(count,),
        in_specs=[tile_of(inputs, inputs_slot), tile_of(upstream, upstream_slot), gain, gain],
        out_specs=[grad_spec, gain, gain],
        out_shape=[
            jax.ShapeDtypeStruct(grad_shape, jnp.bfloat16),
            jax.ShapeDtypeStruct((1, width), jnp.float32),
            jax.ShapeDtypeStruct((1, width), jnp.float32),
        ],
        cost_estimate=pl.CostEstimate(
            flops=flops,
            transcendentals=heads * count * SEQ_LEN * SEQ_LEN,
            bytes_accessed=3 * blocks * half * width * 2,
        ),
        interpret=INTERPRET,
    )(inputs, upstream, gain_qk[None], gain_value[None])
    return grad_in, qk_part[0], value_part[0]


def split_blocks(saved_inputs, incoming):
    parts = lax.axis_size("tp")
    ticks, _, rows, width = saved_inputs.shape
    cut = width // parts
    group = 4 if parts % 4 == 0 else 1
    stacked = saved_inputs.reshape(ticks, rows, width)
    grad = incoming.reshape(rows, width)

    def split_kernel(a_ref, b_ref, c_ref, first_ref, later_ref):
        for j in range(group):
            cols = slice(j * cut, (j + 1) * cut)
            first_ref[j, 0] = a_ref[:, cols]
            first_ref[j, 1] = b_ref[:, cols]
            later_ref[j] = c_ref[:, cols]

    return pl.pallas_call(
        split_kernel,
        grid=(parts // group,),
        in_specs=[
            pl.BlockSpec((None, rows, group * cut), lambda j: (0, 0, j)),
            pl.BlockSpec((rows, group * cut), lambda j: (0, j)),
            pl.BlockSpec((None, rows, group * cut), lambda j: (1, 0, j)),
        ],
        out_specs=[
            pl.BlockSpec((group, 2, rows, cut), lambda j: (j, 0, 0, 0)),
            pl.BlockSpec((group, rows, cut), lambda j: (j, 0, 0)),
        ],
        out_shape=[
            jax.ShapeDtypeStruct((parts, 2, rows, cut), saved_inputs.dtype),
            jax.ShapeDtypeStruct((parts, rows, cut), saved_inputs.dtype),
        ],
        interpret=INTERPRET,
    )(stacked, grad, stacked)


def to_heads(block):
    return lax.all_to_all(block, "tp", 0, 0, tiled=True)


def to_tokens(block):
    back = lax.all_to_all(block, "tp", 0, 0, tiled=True)
    return jnp.transpose(back, (1, 0, 2)).reshape(block.shape[1], -1)


def shards(saved_inputs, incoming, qk_gain, value_gain):
    tick_count = saved_inputs.shape[0]
    local_width = qk_gain.shape[1] // lax.axis_size("tp")
    offset = lax.axis_index("tp") * local_width
    gain_qk = lax.dynamic_slice_in_dim(qk_gain[0], offset, local_width)
    gain_value = lax.dynamic_slice_in_dim(value_gain[0], offset, local_width)
    first, later = split_blocks(saved_inputs, incoming)
    first, gain_qk, gain_value = lax.optimization_barrier((first, gain_qk, gain_value))
    first = to_heads(first)
    grad_in, qk_sum, value_sum = local_backward(first, 0, first, 1, gain_qk, gain_value)
    for t in range(1, tick_count):
        first, later = lax.optimization_barrier((first, later))
        inputs_heads = to_heads(later)
        upstream = pass_on(grad_in)
        grad_in, qk_part, value_part = local_backward(
            inputs_heads, None, upstream, None, gain_qk, gain_value, halves=t == tick_count - 1
        )
        qk_sum = qk_sum + qk_part
        value_sum = value_sum + value_part
    early = to_tokens(pass_on(grad_in[0]))
    late = pass_on(to_tokens(grad_in[1]))
    passed = jnp.concatenate([early, late], axis=0)
    return (passed[None], qk_sum[None], value_sum[None])


def solution(mesh):
    return jax.shard_map(
        shards,
        mesh=mesh,
        in_specs=(
            P(None, "section", "tp", None),
            P("section", "tp", None),
            P("section", None),
            P("section", None),
        ),
        out_specs=(P("section", "tp", None), P("section", "tp"), P("section", "tp")),
        check_vma=False,
    )
```

```python
import functools

import jax
import jax.numpy as jnp
from jax import lax
from jax.sharding import PartitionSpec as P
from jax.experimental import pallas as pl

HEAD_DIM = 128
SEQ_LEN = 256


def from_behind(block, axis, distance):
    devices = range(lax.axis_size(axis))
    route = [((i - distance) % len(devices), i) for i in devices]
    return lax.ppermute(block, axis, route)


def pass_on(grad_in):
    return from_behind(grad_in, "section", -1)


def attend_head(wide, up, gq, gv):
    scale = HEAD_DIM ** (-0.5)
    keys = (wide * gq).astype(jnp.bfloat16)
    values = (wide * gv).astype(jnp.bfloat16)
    nt = (((1,), (1,)), ((), ()))
    tn = (((0,), (0,)), ((), ()))
    scores = lax.dot_general(keys, keys, nt, preferred_element_type=jnp.float32) * scale
    rows = lax.broadcasted_iota(jnp.int32, scores.shape, 0)
    cols = lax.broadcasted_iota(jnp.int32, scores.shape, 1)
    scores = jnp.where(cols <= rows, scores, -jnp.inf)
    row_max = jnp.max(scores, axis=1, keepdims=True)
    weights = jnp.exp(scores - row_max)
    probs = weights / jnp.sum(weights, axis=1, keepdims=True)
    prob_grad = lax.dot_general(up, values, nt, preferred_element_type=jnp.float32)
    score_grad = probs * (prob_grad - jnp.sum(probs * prob_grad, axis=1, keepdims=True))
    score_low = score_grad.astype(jnp.bfloat16)
    probs_low = probs.astype(jnp.bfloat16)
    query_grad = jnp.dot(score_low, keys, preferred_element_type=jnp.float32) * scale
    key_grad = lax.dot_general(score_low, keys, tn, preferred_element_type=jnp.float32) * scale
    value_grad = lax.dot_general(probs_low, up, tn, preferred_element_type=jnp.float32)
    qk_total = query_grad + key_grad
    grad_in = (up.astype(jnp.float32) + qk_total * gq + value_grad * gv).astype(jnp.bfloat16)
    qk_part = jnp.sum(wide * qk_total, axis=0, keepdims=True)
    value_part = jnp.sum(wide * value_grad, axis=0, keepdims=True)
    return grad_in, qk_part, value_part


def attention_kernel(x_ref, u_ref, *refs, split=0):
    n = pl.program_id(0)
    if split:
        ub_ref, gq_ref, gv_ref, g_ref, qs_ref, vs_ref = refs
    else:
        gq_ref, gv_ref, g_ref, qs_ref, vs_ref = refs
    heads = g_ref.shape[-1] // HEAD_DIM
    for h in range(heads):
        cols = slice(h * HEAD_DIM, (h + 1) * HEAD_DIM)
        wide = x_ref[:, :, cols].reshape(SEQ_LEN, HEAD_DIM).astype(jnp.float32)
        up = u_ref[:, :, cols]
        if split:
            up = jnp.where(n < split, up, ub_ref[:, :, cols])
        up = up.reshape(SEQ_LEN, HEAD_DIM)
        grad_in, qk_part, value_part = attend_head(wide, up, gq_ref[:, cols], gv_ref[:, cols])
        if len(g_ref.shape) == 4:
            parts = grad_in.reshape(g_ref.shape[1], g_ref.shape[0], g_ref.shape[2], HEAD_DIM)
            for r in range(g_ref.shape[0]):
                g_ref[r, :, :, cols] = parts[:, r]
        else:
            g_ref[:, :, cols] = grad_in.reshape(g_ref.shape[0], g_ref.shape[1], HEAD_DIM)

        @pl.when(n == 0)
        def _():
            qs_ref[:, cols] = qk_part
            vs_ref[:, cols] = value_part

        @pl.when(n > 0)
        def _():
            qs_ref[:, cols] += qk_part
            vs_ref[:, cols] += value_part


INTERPRET = False


def tile_of(array, slot, base=0):
    half, width = array.shape[-2], array.shape[-1]
    if slot is None:
        return pl.BlockSpec((2, half, width), lambda n: (n + base, 0, 0))
    return pl.BlockSpec((2, None, half, width), lambda n: (n + base, slot, 0, 0))


def local_backward(inputs, inputs_slot, upstream, upstream_slot, gain_qk, gain_value, halves=False,
                   base=0, count=None, upstream_b=None):
    half, width = upstream.shape[-2], upstream.shape[-1]
    heads = width // HEAD_DIM
    if count is None:
        count = inputs.shape[0] * half // SEQ_LEN
    blocks = count * SEQ_LEN // half
    gain = pl.BlockSpec((1, width), lambda n: (0, 0))
    flops = heads * count * 5 * 2 * SEQ_LEN * SEQ_LEN * HEAD_DIM
    if upstream_b is None:
        up_specs = [tile_of(inputs, inputs_slot, base), tile_of(upstream, upstream_slot, base)]
        up_args = (inputs, upstream)
    else:
        last = upstream.shape[0] // 2 - 1
        up_specs = [
            tile_of(inputs, inputs_slot),
            pl.BlockSpec((2, half, width), lambda n: (jnp.minimum(n, last), 0, 0)),
            pl.BlockSpec((2, half, width), lambda n: (jnp.maximum(n - last - 1, 0), 0, 0)),
        ]
        up_args = (inputs, upstream, upstream_b)
    if halves:
        grad_shape = (2, blocks, half // 2, width)
        grad_spec = pl.BlockSpec((2, 2, half // 2, width), lambda n: (0, n, 0, 0))
    else:
        grad_shape = (blocks, half, width)
        grad_spec = tile_of(upstream, None)
    grad_in, qk_part, value_part = pl.pallas_call(
        functools.partial(attention_kernel, split=0 if upstream_b is None else upstream.shape[0] // 2),
        grid=(count,),
        in_specs=up_specs + [gain, gain],
        out_specs=[grad_spec, gain, gain],
        out_shape=[
            jax.ShapeDtypeStruct(grad_shape, jnp.bfloat16),
            jax.ShapeDtypeStruct((1, width), jnp.float32),
            jax.ShapeDtypeStruct((1, width), jnp.float32),
        ],
        cost_estimate=pl.CostEstimate(
            flops=flops,
            transcendentals=heads * count * SEQ_LEN * SEQ_LEN,
            bytes_accessed=3 * blocks * half * width * 2,
        ),
        interpret=INTERPRET,
    )(*up_args, gain_qk[None], gain_value[None])
    return grad_in, qk_part[0], value_part[0]


def split_blocks(saved_inputs, incoming):
    parts = lax.axis_size("tp")
    ticks, _, rows, width = saved_inputs.shape
    cut = width // parts
    group = 4 if parts % 4 == 0 else 1
    stacked = saved_inputs.reshape(ticks, rows, width)
    grad = incoming.reshape(rows, width)

    def split_kernel(a_ref, b_ref, c_ref, first_ref, later_ref):
        for j in range(group):
            cols = slice(j * cut, (j + 1) * cut)
            first_ref[j, 0] = a_ref[:, cols]
            first_ref[j, 1] = b_ref[:, cols]
            later_ref[j] = c_ref[:, cols]

    return pl.pallas_call(
        split_kernel,
        grid=(parts // group,),
        in_specs=[
            pl.BlockSpec((None, rows, group * cut), lambda j: (0, 0, j)),
            pl.BlockSpec((rows, group * cut), lambda j: (0, j)),
            pl.BlockSpec((None, rows, group * cut), lambda j: (1, 0, j)),
        ],
        out_specs=[
            pl.BlockSpec((group, 2, rows, cut), lambda j: (j, 0, 0, 0)),
            pl.BlockSpec((group, rows, cut), lambda j: (j, 0, 0)),
        ],
        out_shape=[
            jax.ShapeDtypeStruct((parts, 2, rows, cut), saved_inputs.dtype),
            jax.ShapeDtypeStruct((parts, rows, cut), saved_inputs.dtype),
        ],
        interpret=INTERPRET,
    )(stacked, grad, stacked)


def to_heads(block):
    return lax.all_to_all(block, "tp", 0, 0, tiled=True)


def to_tokens(block):
    back = lax.all_to_all(block, "tp", 0, 0, tiled=True)
    return jnp.transpose(back, (1, 0, 2)).reshape(block.shape[1], -1)


def shards(saved_inputs, incoming, qk_gain, value_gain):
    tick_count = saved_inputs.shape[0]
    local_width = qk_gain.shape[1] // lax.axis_size("tp")
    offset = lax.axis_index("tp") * local_width
    gain_qk = lax.dynamic_slice_in_dim(qk_gain[0], offset, local_width)
    gain_value = lax.dynamic_slice_in_dim(value_gain[0], offset, local_width)
    first, later = split_blocks(saved_inputs, incoming)
    first, gain_qk, gain_value = lax.optimization_barrier((first, gain_qk, gain_value))
    first = to_heads(first)
    count = first.shape[0] * first.shape[-2] // SEQ_LEN
    part = count // 2
    grad_a, qk_a, value_a = local_backward(first, 0, first, 1, gain_qk, gain_value, base=0, count=part)
    upstream_a = pass_on(grad_a)
    grad_b, qk_b, value_b = local_backward(
        first, 0, first, 1, gain_qk, gain_value, base=part, count=count - part
    )
    upstream_b = pass_on(grad_b)
    qk_sum = qk_a + qk_b
    value_sum = value_a + value_b
    for t in range(1, tick_count):
        first, later = lax.optimization_barrier((first, later))
        inputs_heads = to_heads(later)
        grad_in, qk_part, value_part = local_backward(
            inputs_heads, None, upstream_a, None, gain_qk, gain_value, halves=True, upstream_b=upstream_b
        )
        qk_sum = qk_sum + qk_part
        value_sum = value_sum + value_part
    early = to_tokens(pass_on(grad_in[0]))
    late = pass_on(to_tokens(grad_in[1]))
    passed = jnp.concatenate([early, late], axis=0)
    return (passed[None], qk_sum[None], value_sum[None])


def solution(mesh):
    return jax.shard_map(
        shards,
        mesh=mesh,
        in_specs=(
            P(None, "section", "tp", None),
            P("section", "tp", None),
            P("section", None),
            P("section", None),
        ),
        out_specs=(P("section", "tp", None), P("section", "tp"), P("section", "tp")),
        check_vma=False,
    )
```
